256 devices in a mesh: dp: 16 (over z_lo, x), tensor: 16 (over y, z_hi, core).
Axes of the slice: x: 4, y: 4, z: 8 (z_hi: 2, z_lo: 4; z = z_hi * 4 + z_lo), core: 2. Of those that a mesh axis runs over, the one named last changes fastest.
Arguments:
- inner_x: bfloat16 [16, 2048, 7168], P('dp', None, 'tensor')
- gate_z: bfloat16 [16, 2048, 7168], P('dp', None, 'tensor'), may hold values from -6 to 6
- input_b: bfloat16 [16, 2048, 128], P('dp'), may hold values from -0.75 to 0.75
- output_c: bfloat16 [16, 2048, 128], P('dp'), may hold values from -6 to 6
- step_raw: float32 [16, 2048, 112], P('dp', None, 'tensor'), may hold values from -6 to 6
- decay_rate: float32 [112], P('tensor'), may hold values from 0.001 to 0.05
- skip_gain: float32 [112], P('tensor'), may hold values from 0.5 to 1.5
- norm_gain: float32 [7168], P('tensor'), may hold values from 0.5 to 1.5
- out_weight: bfloat16 [7168, 3584], P('tensor'), may hold values from -0.0625 to 0.0625
- segment: int32 [16, 2048], P('dp'), may hold values from 0 to 7, never falling along the last dimension, each value on 1 to 1024 neighbouring positions
- cache_slot: int32 [16, 8], replicated, may hold values from 0 to 127, as said below
Outputs:
- mixed: bfloat16 [16, 2048, 3584], P('dp', 'tensor')
- cache: float32 [128, 112, 4096], P('dp', 'tensor')
The draws below stay inside these ranges and needn't reach their ends.
Inputs may be any that keep to these rules, and one draw needn't show every extreme that they name: `segment`: in each group's row the prompt numbers never fall and every prompt 0 to 7 is present. `cache_slot`: every slot is named exactly once; slot // 8 is the owning group, and no two prompts of one group have the same owning group.
All inputs are finite; a program needn't handle non-finite values.
Results may differ from the reference program's by a relative error of at most 0.018.
Values may be sent and summed in bfloat16 or wider, within the bound.
No kernel may reach another device: no remote copies, remote signals or barrier semaphores. Data moves between devices by JAX's collectives and lax.ppermute only.
A program may use at most 192 MiB of HBM per device.

```python
import math
import jax
import jax.numpy as jnp
import numpy as np
from jax import lax

D = 3584
HEADS = 112
HEAD = 64
STATE = 64
NGROUPS = 2
REQS = 8
BLOCK = 256
INNER = 7168
GROUPS = 16
STREAM = 2048
SLOTS = 128
N_TENSOR = 16


def draw_inner_x(key, part):
    first_key, second_key, third_key = jax.random.split(key, 3)
    base = jax.random.normal(first_key, (GROUPS, STREAM, INNER), jnp.float32)
    rising = 3.0
    columns = rising ** (jnp.arange(INNER, dtype=jnp.float32) / INNER - 0.5)
    columns = columns * 10.0 ** (jax.random.uniform(second_key, (INNER,), jnp.float32) - 0.5)
    row_scale = 10.0 ** (jax.random.uniform(third_key, (GROUPS, STREAM, 1), jnp.float32) - 0.5)
    return (base * columns[None, None, :] * row_scale).astype(jnp.bfloat16)


def draw_cache_slot(key, part):
    first_key, second_key, third_key = jax.random.split(key, 3)
    drawn = jax.random.permutation(first_key, GROUPS)[:REQS].astype(jnp.int32)
    offsets = (drawn - drawn[0] + GROUPS // 2) % GROUPS
    local_pos = jax.random.permutation(second_key, REQS)
    group_keys = jax.random.split(third_key, GROUPS)
    shuffled = jax.vmap(lambda one_key: jax.random.permutation(one_key, REQS))(group_keys)
    group_ids = jnp.arange(GROUPS, dtype=jnp.int32)[:, None]
    owners = (group_ids + offsets[shuffled]) % GROUPS
    return (owners * REQS + local_pos[shuffled]).astype(jnp.int32)


def level_of(key, extent, pieces, smallest, top_value):
    factor_of = 1.0
    for dim, blocks in pieces:
        draws = jax.random.uniform(jax.random.fold_in(jax.random.fold_in(key, 6), dim), (blocks,), jnp.float32, smallest / len(pieces), top_value / len(pieces))
        factor_of = factor_of * jnp.repeat(jnp.exp(draws), extent[dim] // blocks).reshape((-1,) + (1,) * (len(extent) - 1 - dim))
    return factor_of


def split_up(amount, total, reach, skew):
    weights = [(1 << 20) // math.isqrt(grade ** skew) + 1 for grade in range(2, amount + 1)]
    surplus, counts = total - reach - (amount - 1), [1] * (amount - 1)
    while surplus > 0:
        free = [i for i in range(amount - 1) if counts[i] < reach]
        whole, remaining = sum([weights[i] for i in free]), surplus
        for i in free:
            extra = min(reach - counts[i], max(1, remaining * weights[i] // whole), surplus)
            counts[i] = counts[i] + extra
            surplus = surplus - extra
    return np.array([reach] + counts)


def ragged(stream_key, amount, total, bound, skew):
    if amount == 2:
        one = jax.random.randint(stream_key, (), max(1, total - bound), min(bound, total - 1) + 1)
        return jnp.stack([one, total - one])
    tallies = jnp.asarray(split_up(amount, total, bound, skew), jnp.int32)
    pairs = (amount - 1) // 2
    source_of, taker = tallies[1:1 + 2 * pairs:2], tallies[2:2 + 2 * pairs:2]
    margin = jnp.minimum(source_of - 1, bound - taker)
    moved = jax.random.randint(jax.random.fold_in(stream_key, 1), (pairs,), 0, 1 << 20) % (margin + 1)
    tallies = tallies.at[1:1 + 2 * pairs:2].set(source_of - moved).at[2:2 + 2 * pairs:2].set(taker + moved)
    return tallies[jax.random.permutation(jax.random.fold_in(stream_key, 2), amount)]


def normal_values(own_key, extent, scale, limit, shards=(), kind=jnp.bfloat16):
    values = jax.random.normal(own_key, extent, jnp.float32) * scale
    if len(shards) > 0:
        values = level_of(own_key, extent, shards, -0.22, 0.18) * values
    return jnp.clip(values, min=-limit, max=limit).astype(kind)


def setup_inputs(seed: int = 0) -> dict:
    seeds = jax.random.split(jax.random.key(seed), 12)
    inner_x = draw_inner_x(jax.random.fold_in(seeds[11], 71), 0)
    gate_z = normal_values(seeds[1], (GROUPS, STREAM, INNER), 1.0, 6.0, ((0, 16), (2, 16)))
    input_b = normal_values(seeds[2], (GROUPS, STREAM, NGROUPS * STATE), 0.125, 0.75, ((0, 16),))
    output_c = normal_values(seeds[3], (GROUPS, STREAM, NGROUPS * STATE), 1.0, 6.0, ((0, 16),))
    step_raw = normal_values(seeds[4], (GROUPS, STREAM, HEADS), 1.0, 6.0, ((0, 16), (2, 16)), jnp.float32)
    decay_rate = jnp.clip(jnp.exp(math.log(0.05) - 3.912023 * jax.random.uniform(seeds[5], (HEADS,), jnp.float32) ** level_of(seeds[5], (HEADS,), ((0, 16),), -0.2, 0.2)), 0.001, 0.05)
    skip_gain = jnp.clip(0.5 + 1.0 * jax.random.uniform(seeds[6], (HEADS,), jnp.float32) ** level_of(seeds[6], (HEADS,), ((0, 16),), -0.2, 0.2), 0.5, 1.5)
    norm_gain = jnp.clip(1.0 + 0.1 * jax.random.normal(seeds[7], (INNER,), jnp.float32), 0.5, 1.5)
    out_weight = normal_values(seeds[8], (INNER, D), INNER ** -0.5, 0.0625, ((0, 16),))
    segment = jax.vmap(lambda own: jnp.searchsorted(jnp.cumsum(ragged(own, REQS, STREAM, STREAM // 2, 2)), jnp.arange(STREAM), side="right"))(jax.random.split(seeds[9], GROUPS)).reshape((GROUPS, STREAM)).astype(jnp.int32)
    cache_slot = draw_cache_slot(jax.random.fold_in(seeds[11], 71), 0)
    return dict(inner_x=inner_x, gate_z=gate_z, input_b=input_b, output_c=output_c, step_raw=step_raw, decay_rate=decay_rate, skip_gain=skip_gain, norm_gain=norm_gain, out_weight=out_weight, segment=segment, cache_slot=cache_slot)


HIGHEST = lax.Precision.HIGHEST

def mixer_group(inner_x, gate_z, input_b, output_c, step_raw, seg_row, decay_rate, skip_gain, norm_gain, out_weight):
    stream_len = inner_x.shape[0]
    group_heads = HEADS // NGROUPS
    head_group = jnp.arange(HEADS) // group_heads
    step_size = jax.nn.softplus(step_raw)
    cum_log = jnp.cumsum(-decay_rate[None, :] * step_size, axis=0)
    values = inner_x.astype(jnp.float32).reshape(stream_len, HEADS, HEAD)
    b_float = input_b.astype(jnp.float32).reshape(stream_len, NGROUPS, STATE)
    c_float = output_c.astype(jnp.float32).reshape(stream_len, NGROUPS, STATE)
    block_count = stream_len // BLOCK
    prev_cum = jnp.concatenate([jnp.zeros((1, HEADS), jnp.float32), cum_log[:-1]], axis=0)[::BLOCK]
    prev_seg = jnp.concatenate([jnp.full((1,), -1, seg_row.dtype), seg_row[:-1]], axis=0)[::BLOCK]
    block_inputs = (values.reshape(block_count, BLOCK, HEADS, HEAD), cum_log.reshape(block_count, BLOCK, HEADS), step_size.reshape(block_count, BLOCK, HEADS), seg_row.reshape(block_count, BLOCK), b_float.reshape(block_count, BLOCK, NGROUPS, STATE), c_float.reshape(block_count, BLOCK, NGROUPS, STATE), prev_cum, prev_seg)
    positions = jnp.arange(BLOCK)

    def advance(carried, block_in):
        x_blk, cum_blk, step_blk, seg_blk, b_blk, c_blk, prev_c, prev_s = block_in
        scores = jnp.einsum('tgn,sgn->gts', c_blk, b_blk, precision=HIGHEST)[head_group]
        causal_mask = (positions[None, :] <= positions[:, None]) & (seg_blk[:, None] == seg_blk[None, :])
        log_gap = cum_blk.T[:, :, None] - cum_blk.T[:, None, :]
        weights = jnp.exp(jnp.where(causal_mask[None], log_gap, -jnp.inf)) * step_blk.T[:, None, :] * scores
        intra_part = jnp.einsum('hts,shp->thp', weights, x_blk, precision=HIGHEST)
        live_rows = (seg_blk == prev_s).astype(jnp.float32)
        carry_decay = jnp.exp(cum_blk - prev_c[None, :]) * live_rows[:, None]
        c_heads = c_blk[:, head_group, :]
        carry_part = jnp.einsum('hpn,thn->thp', carried, c_heads, precision=HIGHEST) * carry_decay[:, :, None]
        outputs = intra_part + carry_part + skip_gain[None, :, None] * x_blk
        last_seg = seg_blk[-1]
        last_cum = cum_blk[-1]
        keep_rows = (last_seg == prev_s).astype(jnp.float32)
        pull_back = jnp.exp(last_cum[None, :] - cum_blk) * step_blk * (seg_blk == last_seg).astype(jnp.float32)[:, None]
        b_heads = b_blk[:, head_group, :]
        added_part = jnp.einsum('shp,shn->hpn', pull_back[:, :, None] * x_blk, b_heads, precision=HIGHEST)
        carried = carried * (jnp.exp(last_cum - prev_c) * keep_rows)[:, None, None] + added_part
        return (carried, outputs)
    _, outputs = lax.scan(advance, jnp.zeros((HEADS, HEAD, STATE), jnp.float32), block_inputs)
    mixer_y = outputs.reshape(stream_len, INNER)
    members = (seg_row[None, :] == jnp.arange(REQS)[:, None]).astype(jnp.float32)
    end_index = lax.optimization_barrier(jnp.sum((seg_row[None, :] <= jnp.arange(REQS)[:, None]).astype(jnp.int32), axis=1)) - 1
    at_end = (jnp.arange(stream_len)[None, :] == end_index[:, None]).astype(jnp.float32)
    end_cum = jnp.dot(at_end, cum_log, precision=HIGHEST)
    seg_end_cum = jnp.dot(members.T, end_cum, precision=HIGHEST)
    pull_all = jnp.exp(seg_end_cum - cum_log) * step_size
    weighted = values * pull_all[:, :, None]
    finals_list = []
    for group_idx in range(NGROUPS):
        masked_b = members[:, :, None] * b_float[None, :, group_idx, :]
        group_part = jnp.einsum('thp,rtn->rhpn', weighted[:, group_idx * group_heads:(group_idx + 1) * group_heads], masked_b, precision=HIGHEST)
        finals_list.append(group_part)
    finals = jnp.concatenate(finals_list, axis=1).reshape(REQS, HEADS, HEAD * STATE)
    gated = mixer_y * jax.nn.silu(gate_z.astype(jnp.float32))
    grouped = gated.reshape(stream_len, NGROUPS, INNER // NGROUPS)
    mean_sq = lax.optimization_barrier(jnp.mean(grouped * grouped, axis=-1))
    normed = (grouped * lax.rsqrt(mean_sq + 1e-05)[:, :, None]).reshape(stream_len, INNER) * norm_gain[None, :]
    rounded = normed.astype(jnp.bfloat16)
    dev_width = INNER // N_TENSOR
    blocks_out = (rounded.reshape(stream_len, N_TENSOR, dev_width).transpose(1, 0, 2), out_weight.reshape(N_TENSOR, dev_width, D))

    def accumulate(summed, operands):
        partial_value = jnp.dot(operands[0], operands[1], preferred_element_type=jnp.float32)
        partial_value = lax.optimization_barrier(partial_value.astype(jnp.bfloat16)).astype(jnp.float32)
        return (summed + partial_value, None)
    summed, _ = lax.scan(accumulate, jnp.zeros((stream_len, D), jnp.float32), blocks_out)
    return (summed.astype(jnp.bfloat16), finals)

def reference(inner_x, gate_z, input_b, output_c, step_raw, decay_rate, skip_gain, norm_gain, out_weight, segment, cache_slot):

    def per_group(items):
        return mixer_group(items[0], items[1], items[2], items[3], items[4], items[5], decay_rate, skip_gain, norm_gain, out_weight)
    mixed, finals = lax.map(per_group, (inner_x, gate_z, input_b, output_c, step_raw, segment))
    flat_slots = cache_slot.reshape(-1).astype(jnp.int32)
    cache = jnp.zeros((SLOTS, HEADS, HEAD * STATE), jnp.float32).at[flat_slots].set(finals.reshape(-1, HEADS, HEAD * STATE))
    return (mixed, cache)
```

```python
import jax
import jax.numpy as jnp
from jax import lax
from jax.sharding import PartitionSpec as P

HEADS = 112
HEAD = 64
STATE = 64
NGROUPS = 2
REQS = 8
BLOCK = 256
INNER = 7168


HIGHEST = lax.Precision.HIGHEST


def split_pair(values):
    upper = values.astype(jnp.bfloat16)
    lower = (values - upper.astype(jnp.float32)).astype(jnp.bfloat16)
    return (upper, lower)


def split_einsum(form, wide, narrow):
    upper, lower = split_pair(wide)
    first = jnp.einsum(form, upper, narrow, preferred_element_type=jnp.float32)
    return first + jnp.einsum(form, lower, narrow, preferred_element_type=jnp.float32)


def local(
    inner_x,
    gate_z,
    input_b,
    output_c,
    step_raw,
    decay_rate,
    skip_gain,
    norm_gain,
    out_weight,
    segment,
    cache_slot,
):
    stream_len = inner_x.shape[1]
    dev_width = inner_x.shape[2]
    dev_heads = decay_rate.shape[0]
    tensor_idx = lax.axis_index("tensor")
    group_idx = tensor_idx * dev_heads // (HEADS // NGROUPS)
    b_cols = lax.dynamic_slice_in_dim(input_b[0], group_idx * STATE, STATE, 1)
    c_cols = lax.dynamic_slice_in_dim(output_c[0], group_idx * STATE, STATE, 1)
    step_size = jax.nn.softplus(step_raw[0])
    cum_log = jnp.cumsum(-decay_rate[None, :] * step_size, axis=0)
    seg_row = segment[0]
    block_count = stream_len // BLOCK
    x_blk = inner_x[0].reshape(block_count, BLOCK, dev_heads, HEAD)
    cum_blk = cum_log.reshape(block_count, BLOCK, dev_heads)
    step_blk = step_size.reshape(block_count, BLOCK, dev_heads)
    seg_blk = seg_row.reshape(block_count, BLOCK)
    b_blk = b_cols.reshape(block_count, BLOCK, STATE)
    c_blk = c_cols.reshape(block_count, BLOCK, STATE)
    positions = jnp.arange(BLOCK)
    scores = jnp.einsum("btn,bsn->bts", c_blk, b_blk, preferred_element_type=jnp.float32)
    causal_mask = (positions[None, None, :] <= positions[None, :, None]) & (
        seg_blk[:, :, None] == seg_blk[:, None, :]
    )
    cum_t = cum_blk.transpose(0, 2, 1)
    log_gap = cum_t[:, :, :, None] - cum_t[:, :, None, :]
    weights = (
        jnp.exp(jnp.where(causal_mask[:, None], log_gap, -jnp.inf))
        * step_blk.transpose(0, 2, 1)[:, :, None, :]
        * scores[:, None]
    )
    intra_part = split_einsum("bhts,bshp->bthp", weights, x_blk)
    last_seg = seg_blk[:, -1]
    last_cum = cum_blk[:, -1]
    pull_back = (
        jnp.exp(last_cum[:, None, :] - cum_blk)
        * step_blk
        * (seg_blk == last_seg[:, None]).astype(jnp.float32)[:, :, None]
    )
    added = split_einsum("bshp,bsn->bhpn", pull_back[:, :, :, None] * x_blk, b_blk)
    prev_cum = jnp.concatenate([jnp.zeros((1, dev_heads), jnp.float32), last_cum[:-1]], axis=0)
    prev_seg = jnp.concatenate([jnp.full((1,), -1, seg_row.dtype), last_seg[:-1]], axis=0)
    blocks = jnp.arange(block_count)
    earlier = blocks[None, :] < blocks[:, None]
    mix_ok = earlier & (last_seg[None, :] == prev_seg[:, None])
    mix_gap = prev_cum[:, None, :] - last_cum[None, :, :]
    mix = jnp.exp(jnp.where(mix_ok[:, :, None], mix_gap, -jnp.inf))
    carried = jnp.sum(mix[:, :, :, None, None] * added[None], axis=1)
    live_rows = (seg_blk == prev_seg[:, None]).astype(jnp.float32)
    carry_decay = jnp.exp(cum_blk - prev_cum[:, None, :]) * live_rows[:, :, None]
    carry_part = split_einsum("bhpn,btn->bthp", carried, c_blk) * carry_decay[:, :, :, None]
    outputs = intra_part + carry_part + skip_gain[None, None, :, None] * x_blk.astype(jnp.float32)
    mixer_y = outputs.reshape(stream_len, dev_width)
    members = (seg_row[None, :] == jnp.arange(REQS)[:, None]).astype(jnp.float32)
    end_index = (
        jnp.sum((seg_row[None, :] <= jnp.arange(REQS)[:, None]).astype(jnp.int32), axis=1) - 1
    )
    at_end = (jnp.arange(stream_len)[None, :] == end_index[:, None]).astype(jnp.float32)
    end_cum = jnp.dot(at_end, cum_log, precision=HIGHEST)
    seg_end_cum = jnp.dot(members.T, end_cum, precision=HIGHEST)
    pull_all = jnp.exp(seg_end_cum - cum_log) * step_size
    weighted = (inner_x[0].reshape(stream_len, dev_heads, HEAD) * pull_all[:, :, None]).reshape(
        stream_len, dev_width
    )
    masked_b = (
        (members.astype(jnp.bfloat16)[:, :, None] * b_cols[None])
        .transpose(1, 0, 2)
        .reshape(stream_len, REQS * STATE)
    )
    finals = split_einsum("tc,tk->ck", weighted, masked_b)
    finals = (
        finals.reshape(dev_heads, HEAD, REQS, STATE)
        .transpose(2, 0, 1, 3)
        .reshape(REQS, dev_heads * HEAD * STATE)
    )
    gated = mixer_y * jax.nn.silu(gate_z[0].astype(jnp.float32))
    sum_sq = jnp.sum(gated * gated, axis=1)
    group_hot = (jnp.arange(NGROUPS) == group_idx).astype(jnp.float32)
    group_stat = lax.psum(sum_sq[:, None] * group_hot[None, :], "tensor")
    mean_sq = jnp.sum(group_stat * group_hot[None, :], axis=1) / (INNER // NGROUPS)
    rounded = (gated * lax.rsqrt(mean_sq + 1e-05)[:, None] * norm_gain[None, :]).astype(
        jnp.bfloat16
    )
    projected = lax.psum_scatter(
        jnp.dot(rounded, out_weight, preferred_element_type=jnp.float32).astype(jnp.bfloat16),
        "tensor",
        scatter_dimension=0,
        tiled=True,
    )
    mixed = projected[None]
    dp_idx = lax.axis_index("dp")
    dp_size = lax.axis_size("dp")
    own_slots = lax.dynamic_slice_in_dim(cache_slot, dp_idx, 1, 0)[0]
    dest_hot = ((own_slots // REQS)[:, None] == jnp.arange(dp_size)[None, :]).astype(jnp.float32)
    outbound = jnp.dot(dest_hot.T, finals, precision=HIGHEST).reshape(
        dp_size, dev_heads, HEAD * STATE
    )
    inbound = lax.all_to_all(
        outbound.astype(jnp.bfloat16), "dp", split_axis=0, concat_axis=0, tiled=True
    ).astype(outbound.dtype)
    wanted = dp_idx * REQS + jnp.arange(REQS)
    take_hot = jnp.any(cache_slot[:, :, None] == wanted[None, None, :], axis=1).astype(jnp.float32)
    cache = jnp.dot(
        take_hot.T, inbound.reshape(dp_size, dev_heads * HEAD * STATE), precision=HIGHEST
    )
    return (mixed, cache.reshape(REQS, dev_heads, HEAD * STATE))


def solution(mesh):
    in_specs = (
        P("dp", None, "tensor"),
        P("dp", None, "tensor"),
        P("dp", None, None),
        P("dp", None, None),
        P("dp", None, "tensor"),
        P("tensor"),
        P("tensor"),
        P("tensor"),
        P("tensor", None),
        P("dp", None),
        P(),
    )
    out_specs = (P("dp", "tensor", None), P("dp", "tensor", None))
    return jax.shard_map(local, mesh=mesh, in_specs=in_specs, out_specs=out_specs, check_vma=False)
```

```python
import jax
import jax.numpy as jnp
from jax import lax
from jax.sharding import Mesh, PartitionSpec as P

HEADS = 112
HEAD = 64
STATE = 64
NGROUPS = 2
REQS = 8
BLOCK = 256
INNER = 7168


HIGHEST = lax.Precision.HIGHEST
TENSOR = ("head_group", "y_rest", "z_hi", "core")
GROUP_MATES = TENSOR[1:]


def split_pair(values):
    upper = values.astype(jnp.bfloat16)
    lower = (values - upper.astype(jnp.float32)).astype(jnp.bfloat16)
    return (upper, lower)


def split_einsum(form, wide, narrow):
    upper, lower = split_pair(wide)
    first = jnp.einsum(form, upper, narrow, preferred_element_type=jnp.float32)
    return first + jnp.einsum(form, lower, narrow, preferred_element_type=jnp.float32)


def local(
    inner_x,
    gate_z,
    input_b,
    output_c,
    step_raw,
    decay_rate,
    skip_gain,
    norm_gain,
    out_weight,
    segment,
    cache_slot,
):
    stream_len = inner_x.shape[1]
    dev_width = inner_x.shape[2]
    dev_heads = decay_rate.shape[0]
    tensor_idx = lax.axis_index(TENSOR)
    group_idx = tensor_idx * dev_heads // (HEADS // NGROUPS)
    b_cols = lax.dynamic_slice_in_dim(input_b[0], group_idx * STATE, STATE, 1)
    c_cols = lax.dynamic_slice_in_dim(output_c[0], group_idx * STATE, STATE, 1)
    step_size = jax.nn.softplus(step_raw[0])
    cum_log = jnp.cumsum(-decay_rate[None, :] * step_size, axis=0)
    seg_row = segment[0]
    block_count = stream_len // BLOCK
    x_blk = inner_x[0].reshape(block_count, BLOCK, dev_heads, HEAD)
    cum_blk = cum_log.reshape(block_count, BLOCK, dev_heads)
    step_blk = step_size.reshape(block_count, BLOCK, dev_heads)
    seg_blk = seg_row.reshape(block_count, BLOCK)
    b_blk = b_cols.reshape(block_count, BLOCK, STATE)
    c_blk = c_cols.reshape(block_count, BLOCK, STATE)
    positions = jnp.arange(BLOCK)
    scores = jnp.einsum("btn,bsn->bts", c_blk, b_blk, preferred_element_type=jnp.float32)
    causal_mask = (positions[None, None, :] <= positions[None, :, None]) & (
        seg_blk[:, :, None] == seg_blk[:, None, :]
    )
    cum_t = cum_blk.transpose(0, 2, 1)
    log_gap = cum_t[:, :, :, None] - cum_t[:, :, None, :]
    weights = (
        jnp.exp(jnp.where(causal_mask[:, None], log_gap, -jnp.inf))
        * step_blk.transpose(0, 2, 1)[:, :, None, :]
        * scores[:, None]
    )
    intra_part = split_einsum("bhts,bshp->bthp", weights, x_blk)
    last_seg = seg_blk[:, -1]
    last_cum = cum_blk[:, -1]
    pull_back = (
        jnp.exp(last_cum[:, None, :] - cum_blk)
        * step_blk
        * (seg_blk == last_seg[:, None]).astype(jnp.float32)[:, :, None]
    )
    added = split_einsum("bshp,bsn->bhpn", pull_back[:, :, :, None] * x_blk, b_blk)
    prev_cum = jnp.concatenate([jnp.zeros((1, dev_heads), jnp.float32), last_cum[:-1]], axis=0)
    prev_seg = jnp.concatenate([jnp.full((1,), -1, seg_row.dtype), last_seg[:-1]], axis=0)
    blocks = jnp.arange(block_count)
    earlier = blocks[None, :] < blocks[:, None]
    mix_ok = earlier & (last_seg[None, :] == prev_seg[:, None])
    mix_gap = prev_cum[:, None, :] - last_cum[None, :, :]
    mix = jnp.exp(jnp.where(mix_ok[:, :, None], mix_gap, -jnp.inf))
    carried = jnp.sum(mix[:, :, :, None, None] * added[None], axis=1)
    live_rows = (seg_blk == prev_seg[:, None]).astype(jnp.float32)
    carry_decay = jnp.exp(cum_blk - prev_cum[:, None, :]) * live_rows[:, :, None]
    carry_part = split_einsum("bhpn,btn->bthp", carried, c_blk) * carry_decay[:, :, :, None]
    outputs = intra_part + carry_part + skip_gain[None, None, :, None] * x_blk.astype(jnp.float32)
    mixer_y = outputs.reshape(stream_len, dev_width)
    members = (seg_row[None, :] == jnp.arange(REQS)[:, None]).astype(jnp.float32)
    end_index = (
        jnp.sum((seg_row[None, :] <= jnp.arange(REQS)[:, None]).astype(jnp.int32), axis=1) - 1
    )
    at_end = (jnp.arange(stream_len)[None, :] == end_index[:, None]).astype(jnp.float32)
    end_cum = jnp.dot(at_end, cum_log, precision=HIGHEST)
    seg_end_cum = jnp.dot(members.T, end_cum, precision=HIGHEST)
    pull_all = jnp.exp(seg_end_cum - cum_log) * step_size
    weighted = (inner_x[0].reshape(stream_len, dev_heads, HEAD) * pull_all[:, :, None]).reshape(
        stream_len, dev_width
    )
    masked_b = (
        (members.astype(jnp.bfloat16)[:, :, None] * b_cols[None])
        .transpose(1, 0, 2)
        .reshape(stream_len, REQS * STATE)
    )
    finals = split_einsum("tc,tk->ck", weighted, masked_b)
    finals = (
        finals.reshape(dev_heads, HEAD, REQS, STATE)
        .transpose(2, 0, 1, 3)
        .reshape(REQS, dev_heads * HEAD * STATE)
    )
    gated = mixer_y * jax.nn.silu(gate_z[0].astype(jnp.float32))
    sum_sq = jnp.sum(gated * gated, axis=1)
    group_stat = lax.all_gather(sum_sq, GROUP_MATES, tiled=True)
    mean_sq = jnp.sum(group_stat.reshape(-1, stream_len), axis=0) / (INNER // NGROUPS)
    rounded = (gated * lax.rsqrt(mean_sq + 1e-05)[:, None] * norm_gain[None, :]).astype(
        jnp.bfloat16
    )
    projected = lax.psum_scatter(
        jnp.dot(rounded, out_weight, preferred_element_type=jnp.float32).astype(jnp.bfloat16),
        TENSOR,
        scatter_dimension=0,
        tiled=True,
    )
    mixed = projected[None]
    dp_idx = lax.axis_index("dp")
    dp_size = lax.axis_size("dp")
    own_slots = lax.dynamic_slice_in_dim(cache_slot, dp_idx, 1, 0)[0]
    dest_hot = ((own_slots // REQS)[:, None] == jnp.arange(dp_size)[None, :]).astype(jnp.float32)
    outbound = jnp.dot(dest_hot.T, finals, precision=HIGHEST).reshape(
        dp_size, dev_heads, HEAD * STATE
    )
    inbound = lax.all_to_all(
        outbound.astype(jnp.bfloat16), "dp", split_axis=0, concat_axis=0, tiled=True
    ).astype(outbound.dtype)
    wanted = dp_idx * REQS + jnp.arange(REQS)
    take_hot = jnp.any(cache_slot[:, :, None] == wanted[None, None, :], axis=1).astype(jnp.float32)
    cache = jnp.dot(
        take_hot.T, inbound.reshape(dp_size, dev_heads * HEAD * STATE), precision=HIGHEST
    )
    return (mixed, cache.reshape(REQS, dev_heads, HEAD * STATE))


def solution(mesh):
    dp_size, tensor_size = mesh.devices.shape
    groups = NGROUPS
    rest = tensor_size // (2 * 2 * groups)
    split = Mesh(
        mesh.devices.reshape(dp_size, groups, rest, 2, 2), ("dp",) + TENSOR
    )
    tp = TENSOR
    in_specs = (
        P("dp", None, tp),
        P("dp", None, tp),
        P("dp", None, None),
        P("dp", None, None),
        P("dp", None, tp),
        P(tp),
        P(tp),
        P(tp),
        P(tp, None),
        P("dp", None),
        P(),
    )
    out_specs = (P("dp", tp, None), P("dp", tp, None))
    return jax.shard_map(local, mesh=split, in_specs=in_specs, out_specs=out_specs, check_vma=False)
```

```python
import jax
import jax.numpy as jnp
from jax import lax
from jax.sharding import Mesh, PartitionSpec as P

HEADS = 112
HEAD = 64
STATE = 64
NGROUPS = 2
REQS = 8
BLOCK = 256
INNER = 7168


HIGHEST = lax.Precision.HIGHEST
TENSOR = ("head_group", "y_rest", "z_hi", "core")
GROUP_MATES = TENSOR[1:]
NEAR_FIRST = ("head_group", "y_rest", "core")
FAR_LAST = "z_hi"


def split_pair(values):
    upper = values.astype(jnp.bfloat16)
    lower = (values - upper.astype(jnp.float32)).astype(jnp.bfloat16)
    return (upper, lower)


def split_einsum(form, wide, narrow):
    upper, lower = split_pair(wide)
    first = jnp.einsum(form, upper, narrow, preferred_element_type=jnp.float32)
    return first + jnp.einsum(form, lower, narrow, preferred_element_type=jnp.float32)


def local(
    inner_x,
    gate_z,
    input_b,
    output_c,
    step_raw,
    decay_rate,
    skip_gain,
    norm_gain,
    out_weight,
    segment,
    cache_slot,
):
    stream_len = inner_x.shape[1]
    dev_width = inner_x.shape[2]
    dev_heads = decay_rate.shape[0]
    tensor_idx = lax.axis_index(TENSOR)
    group_idx = tensor_idx * dev_heads // (HEADS // NGROUPS)
    b_cols = lax.dynamic_slice_in_dim(input_b[0], group_idx * STATE, STATE, 1)
    c_cols = lax.dynamic_slice_in_dim(output_c[0], group_idx * STATE, STATE, 1)
    step_size = jax.nn.softplus(step_raw[0])
    cum_log = jnp.cumsum(-decay_rate[None, :] * step_size, axis=0)
    seg_row = segment[0]
    block_count = stream_len // BLOCK
    x_blk = inner_x[0].reshape(block_count, BLOCK, dev_heads, HEAD)
    cum_blk = cum_log.reshape(block_count, BLOCK, dev_heads)
    step_blk = step_size.reshape(block_count, BLOCK, dev_heads)
    seg_blk = seg_row.reshape(block_count, BLOCK)
    b_blk = b_cols.reshape(block_count, BLOCK, STATE)
    c_blk = c_cols.reshape(block_count, BLOCK, STATE)
    positions = jnp.arange(BLOCK)
    scores = jnp.einsum("btn,bsn->bts", c_blk, b_blk, preferred_element_type=jnp.float32)
    causal_mask = (positions[None, None, :] <= positions[None, :, None]) & (
        seg_blk[:, :, None] == seg_blk[:, None, :]
    )
    cum_t = cum_blk.transpose(0, 2, 1)
    log_gap = cum_t[:, :, :, None] - cum_t[:, :, None, :]
    weights = (
        jnp.exp(jnp.where(causal_mask[:, None], log_gap, -jnp.inf))
        * step_blk.transpose(0, 2, 1)[:, :, None, :]
        * scores[:, None]
    )
    intra_part = split_einsum("bhts,bshp->bthp", weights, x_blk)
    last_seg = seg_blk[:, -1]
    last_cum = cum_blk[:, -1]
    pull_back = (
        jnp.exp(last_cum[:, None, :] - cum_blk)
        * step_blk
        * (seg_blk == last_seg[:, None]).astype(jnp.float32)[:, :, None]
    )
    added = split_einsum("bshp,bsn->bhpn", pull_back[:, :, :, None] * x_blk, b_blk)
    prev_cum = jnp.concatenate([jnp.zeros((1, dev_heads), jnp.float32), last_cum[:-1]], axis=0)
    prev_seg = jnp.concatenate([jnp.full((1,), -1, seg_row.dtype), last_seg[:-1]], axis=0)
    blocks = jnp.arange(block_count)
    earlier = blocks[None, :] < blocks[:, None]
    mix_ok = earlier & (last_seg[None, :] == prev_seg[:, None])
    mix_gap = prev_cum[:, None, :] - last_cum[None, :, :]
    mix = jnp.exp(jnp.where(mix_ok[:, :, None], mix_gap, -jnp.inf))
    carried = jnp.sum(mix[:, :, :, None, None] * added[None], axis=1)
    live_rows = (seg_blk == prev_seg[:, None]).astype(jnp.float32)
    carry_decay = jnp.exp(cum_blk - prev_cum[:, None, :]) * live_rows[:, :, None]
    carry_part = split_einsum("bhpn,btn->bthp", carried, c_blk) * carry_decay[:, :, :, None]
    outputs = intra_part + carry_part + skip_gain[None, None, :, None] * x_blk.astype(jnp.float32)
    mixer_y = outputs.reshape(stream_len, dev_width)
    members = (seg_row[None, :] == jnp.arange(REQS)[:, None]).astype(jnp.float32)
    end_index = (
        jnp.sum((seg_row[None, :] <= jnp.arange(REQS)[:, None]).astype(jnp.int32), axis=1) - 1
    )
    at_end = (jnp.arange(stream_len)[None, :] == end_index[:, None]).astype(jnp.float32)
    end_cum = jnp.dot(at_end, cum_log, precision=HIGHEST)
    seg_end_cum = jnp.dot(members.T, end_cum, precision=HIGHEST)
    pull_all = jnp.exp(seg_end_cum - cum_log) * step_size
    weighted = (inner_x[0].reshape(stream_len, dev_heads, HEAD) * pull_all[:, :, None]).reshape(
        stream_len, dev_width
    )
    masked_b = (
        (members.astype(jnp.bfloat16)[:, :, None] * b_cols[None])
        .transpose(1, 0, 2)
        .reshape(stream_len, REQS * STATE)
    )
    finals = split_einsum("tc,tk->ck", weighted, masked_b)
    finals = (
        finals.reshape(dev_heads, HEAD, REQS, STATE)
        .transpose(2, 0, 1, 3)
        .reshape(REQS, dev_heads * HEAD * STATE)
    )
    gated = mixer_y * jax.nn.silu(gate_z[0].astype(jnp.float32))
    sum_sq = jnp.sum(gated * gated, axis=1)
    group_stat = lax.all_gather(sum_sq, GROUP_MATES, tiled=True)
    mean_sq = jnp.sum(group_stat.reshape(-1, stream_len), axis=0) / (INNER // NGROUPS)
    rounded = (gated * lax.rsqrt(mean_sq + 1e-05)[:, None] * norm_gain[None, :]).astype(
        jnp.bfloat16
    )
    sizes = [lax.axis_size(name) for name in TENSOR]
    rows = stream_len // (sizes[0] * sizes[1] * sizes[2] * sizes[3])
    reordered = (
        rounded.reshape(sizes[0], sizes[1], sizes[2], sizes[3], rows, dev_width)
        .transpose(0, 1, 3, 2, 4, 5)
        .reshape(stream_len, dev_width)
    )
    partial = jnp.dot(reordered, out_weight, preferred_element_type=jnp.float32).astype(jnp.bfloat16)
    near = lax.psum_scatter(partial, NEAR_FIRST, scatter_dimension=0, tiled=True)
    projected = lax.psum_scatter(near, FAR_LAST, scatter_dimension=0, tiled=True)
    mixed = projected[None]
    dp_idx = lax.axis_index("dp")
    dp_size = lax.axis_size("dp")
    own_slots = lax.dynamic_slice_in_dim(cache_slot, dp_idx, 1, 0)[0]
    dest_hot = ((own_slots // REQS)[:, None] == jnp.arange(dp_size)[None, :]).astype(jnp.float32)
    outbound = jnp.dot(dest_hot.T, finals, precision=HIGHEST).reshape(
        dp_size, dev_heads, HEAD * STATE
    )
    inbound = lax.all_to_all(
        outbound.astype(jnp.bfloat16), "dp", split_axis=0, concat_axis=0, tiled=True
    ).astype(outbound.dtype)
    wanted = dp_idx * REQS + jnp.arange(REQS)
    take_hot = jnp.any(cache_slot[:, :, None] == wanted[None, None, :], axis=1).astype(jnp.float32)
    cache = jnp.dot(
        take_hot.T, inbound.reshape(dp_size, dev_heads * HEAD * STATE), precision=HIGHEST
    )
    return (mixed, cache.reshape(REQS, dev_heads, HEAD * STATE))


def solution(mesh):
    dp_size, tensor_size = mesh.devices.shape
    groups = NGROUPS
    rest = tensor_size // (2 * 2 * groups)
    split = Mesh(
        mesh.devices.reshape(dp_size, groups, rest, 2, 2), ("dp",) + TENSOR
    )
    tp = TENSOR
    in_specs = (
        P("dp", None, tp),
        P("dp", None, tp),
        P("dp", None, None),
        P("dp", None, None),
        P("dp", None, tp),
        P(tp),
        P(tp),
        P(tp),
        P(tp, None),
        P("dp", None),
        P(),
    )
    out_specs = (P("dp", tp, None), P("dp", tp, None))
    return jax.shard_map(local, mesh=split, in_specs=in_specs, out_specs=out_specs, check_vma=False)
```

```python
import jax
import jax.numpy as jnp
from jax import lax
from jax.sharding import Mesh, PartitionSpec as P

HEADS = 112
HEAD = 64
STATE = 64
NGROUPS = 2
REQS = 8
BLOCK = 256
INNER = 7168


HIGHEST = lax.Precision.HIGHEST
TENSOR = ("head_group", "y_rest", "z_hi", "core")
GROUP_MATES = TENSOR[1:]
NEAR_FIRST = ("head_group", "y_rest", "core")
FAR_LAST = "z_hi"


def split_pair(values):
    upper = values.astype(jnp.bfloat16)
    lower = (values - upper.astype(jnp.float32)).astype(jnp.bfloat16)
    return (upper, lower)


def split_einsum(form, wide, narrow):
    upper, lower = split_pair(wide)
    first = jnp.einsum(form, upper, narrow, preferred_element_type=jnp.float32)
    return first + jnp.einsum(form, lower, narrow, preferred_element_type=jnp.float32)


def local(
    inner_x,
    gate_z,
    input_b,
    output_c,
    step_raw,
    decay_rate,
    skip_gain,
    norm_gain,
    out_weight,
    segment,
    cache_slot,
):
    stream_len = inner_x.shape[1]
    dev_width = inner_x.shape[2]
    dev_heads = decay_rate.shape[0]
    tensor_idx = lax.axis_index(TENSOR)
    group_idx = tensor_idx * dev_heads // (HEADS // NGROUPS)
    b_cols = lax.dynamic_slice_in_dim(input_b[0], group_idx * STATE, STATE, 1)
    c_cols = lax.dynamic_slice_in_dim(output_c[0], group_idx * STATE, STATE, 1)
    step_size = jax.nn.softplus(step_raw[0])
    cum_log = jnp.cumsum(-decay_rate[None, :] * step_size, axis=0)
    seg_row = segment[0]
    block_count = stream_len // BLOCK
    x_blk = inner_x[0].reshape(block_count, BLOCK, dev_heads, HEAD)
    cum_blk = cum_log.reshape(block_count, BLOCK, dev_heads)
    step_blk = step_size.reshape(block_count, BLOCK, dev_heads)
    seg_blk = seg_row.reshape(block_count, BLOCK)
    b_blk = b_cols.reshape(block_count, BLOCK, STATE)
    c_blk = c_cols.reshape(block_count, BLOCK, STATE)
    positions = jnp.arange(BLOCK)
    scores = jnp.einsum("btn,bsn->bts", c_blk, b_blk, preferred_element_type=jnp.float32)
    causal_mask = (positions[None, None, :] <= positions[None, :, None]) & (
        seg_blk[:, :, None] == seg_blk[:, None, :]
    )
    cum_t = cum_blk.transpose(0, 2, 1)
    log_gap = cum_t[:, :, :, None] - cum_t[:, :, None, :]
    weights = (
        jnp.exp(jnp.where(causal_mask[:, None], log_gap, -jnp.inf))
        * step_blk.transpose(0, 2, 1)[:, :, None, :]
        * scores[:, None]
    )
    intra_part = split_einsum("bhts,bshp->bthp", weights, x_blk)
    last_seg = seg_blk[:, -1]
    last_cum = cum_blk[:, -1]
    pull_back = (
        jnp.exp(last_cum[:, None, :] - cum_blk)
        * step_blk
        * (seg_blk == last_seg[:, None]).astype(jnp.float32)[:, :, None]
    )
    added = split_einsum("bshp,bsn->bhpn", pull_back[:, :, :, None] * x_blk, b_blk)
    prev_cum = jnp.concatenate([jnp.zeros((1, dev_heads), jnp.float32), last_cum[:-1]], axis=0)
    prev_seg = jnp.concatenate([jnp.full((1,), -1, seg_row.dtype), last_seg[:-1]], axis=0)
    blocks = jnp.arange(block_count)
    earlier = blocks[None, :] < blocks[:, None]
    mix_ok = earlier & (last_seg[None, :] == prev_seg[:, None])
    mix_gap = prev_cum[:, None, :] - last_cum[None, :, :]
    mix = jnp.exp(jnp.where(mix_ok[:, :, None], mix_gap, -jnp.inf))
    carried = jnp.sum(mix[:, :, :, None, None] * added[None], axis=1)
    live_rows = (seg_blk == prev_seg[:, None]).astype(jnp.float32)
    carry_decay = jnp.exp(cum_blk - prev_cum[:, None, :]) * live_rows[:, :, None]
    carry_part = split_einsum("bhpn,btn->bthp", carried, c_blk) * carry_decay[:, :, :, None]
    outputs = intra_part + carry_part + skip_gain[None, None, :, None] * x_blk.astype(jnp.float32)
    mixer_y = outputs.reshape(stream_len, dev_width)
    members = (seg_row[None, :] == jnp.arange(REQS)[:, None]).astype(jnp.float32)
    end_index = (
        jnp.sum((seg_row[None, :] <= jnp.arange(REQS)[:, None]).astype(jnp.int32), axis=1) - 1
    )
    at_end = (jnp.arange(stream_len)[None, :] == end_index[:, None]).astype(jnp.float32)
    end_cum = jnp.dot(at_end, cum_log, precision=HIGHEST)
    seg_end_cum = jnp.dot(members.T, end_cum, precision=HIGHEST)
    pull_all = jnp.exp(seg_end_cum - cum_log) * step_size
    weighted = (inner_x[0].reshape(stream_len, dev_heads, HEAD) * pull_all[:, :, None]).reshape(
        stream_len, dev_width
    )
    masked_b = (
        (members.astype(jnp.bfloat16)[:, :, None] * b_cols[None])
        .transpose(1, 0, 2)
        .reshape(stream_len, REQS * STATE)
    )
    finals = split_einsum("tc,tk->ck", weighted, masked_b)
    finals = (
        finals.reshape(dev_heads, HEAD, REQS, STATE)
        .transpose(2, 0, 1, 3)
        .reshape(REQS, dev_heads * HEAD * STATE)
    )
    gated = mixer_y * jax.nn.silu(gate_z[0].astype(jnp.float32))
    sum_sq = jnp.sum(gated * gated, axis=1)
    group_stat = lax.all_gather(sum_sq, GROUP_MATES, tiled=True)
    mean_sq = jnp.sum(group_stat.reshape(-1, stream_len), axis=0) / (INNER // NGROUPS)
    rounded = (gated * lax.rsqrt(mean_sq + 1e-05)[:, None] * norm_gain[None, :]).astype(
        jnp.bfloat16
    )
    sizes = [lax.axis_size(name) for name in TENSOR]
    rows = stream_len // (sizes[0] * sizes[1] * sizes[2] * sizes[3])
    reordered = (
        rounded.reshape(sizes[0], sizes[1], sizes[2], sizes[3], rows, dev_width)
        .transpose(0, 1, 3, 2, 4, 5)
        .reshape(stream_len, dev_width)
    )
    partial = jnp.dot(reordered, out_weight, preferred_element_type=jnp.float32).astype(jnp.bfloat16)
    near = lax.psum_scatter(partial, NEAR_FIRST, scatter_dimension=0, tiled=True)
    mixed = near
    dp_idx = lax.axis_index("dp")
    dp_size = lax.axis_size("dp")
    own_slots = lax.dynamic_slice_in_dim(cache_slot, dp_idx, 1, 0)[0]
    dest_hot = ((own_slots // REQS)[:, None] == jnp.arange(dp_size)[None, :]).astype(jnp.float32)
    outbound = jnp.dot(dest_hot.T, finals, precision=HIGHEST).reshape(
        dp_size, dev_heads, HEAD * STATE
    )
    inbound = lax.all_to_all(
        outbound.astype(jnp.bfloat16), "dp", split_axis=0, concat_axis=0, tiled=True
    ).astype(outbound.dtype)
    near, inbound = lax.optimization_barrier((mixed, inbound))
    projected = lax.psum_scatter(near, FAR_LAST, scatter_dimension=0, tiled=True)
    mixed = projected[None]
    wanted = dp_idx * REQS + jnp.arange(REQS)
    take_hot = jnp.any(cache_slot[:, :, None] == wanted[None, None, :], axis=1).astype(jnp.float32)
    cache = jnp.dot(
        take_hot.T, inbound.reshape(dp_size, dev_heads * HEAD * STATE), precision=HIGHEST
    )
    return (mixed, cache.reshape(REQS, dev_heads, HEAD * STATE))


def solution(mesh):
    dp_size, tensor_size = mesh.devices.shape
    groups = NGROUPS
    rest = tensor_size // (2 * 2 * groups)
    split = Mesh(
        mesh.devices.reshape(dp_size, groups, rest, 2, 2), ("dp",) + TENSOR
    )
    tp = TENSOR
    in_specs = (
        P("dp", None, tp),
        P("dp", None, tp),
        P("dp", None, None),
        P("dp", None, None),
        P("dp", None, tp),
        P(tp),
        P(tp),
        P(tp),
        P(tp, None),
        P("dp", None),
        P(),
    )
    out_specs = (P("dp", tp, None), P("dp", tp, None))
    return jax.shard_map(local, mesh=split, in_specs=in_specs, out_specs=out_specs, check_vma=False)
```

```python
import jax
import jax.numpy as jnp
from jax import lax
from jax.sharding import Mesh, PartitionSpec as P

HEADS = 112
HEAD = 64
STATE = 64
NGROUPS = 2
REQS = 8
BLOCK = 256
INNER = 7168


HIGHEST = lax.Precision.HIGHEST
TENSOR = ("head_group", "y_rest", "z_hi", "core")
GROUP_MATES = TENSOR[1:]
NEAR_FIRST = ("head_group", "y_rest", "core")
FAR_LAST = "z_hi"


def split_pair(values):
    upper = values.astype(jnp.bfloat16)
    lower = (values - upper.astype(jnp.float32)).astype(jnp.bfloat16)
    return (upper, lower)


def split_einsum(form, wide, narrow):
    upper, lower = split_pair(wide)
    first = jnp.einsum(form, upper, narrow, preferred_element_type=jnp.float32)
    return first + jnp.einsum(form, lower, narrow, preferred_element_type=jnp.float32)


def local(
    inner_x,
    gate_z,
    input_b,
    output_c,
    step_raw,
    decay_rate,
    skip_gain,
    norm_gain,
    out_weight,
    segment,
    cache_slot,
):
    stream_len = inner_x.shape[1]
    dev_width = inner_x.shape[2]
    dev_heads = decay_rate.shape[0]
    tensor_idx = lax.axis_index(TENSOR)
    group_idx = tensor_idx * dev_heads // (HEADS // NGROUPS)
    b_cols = lax.dynamic_slice_in_dim(input_b[0], group_idx * STATE, STATE, 1)
    c_cols = lax.dynamic_slice_in_dim(output_c[0], group_idx * STATE, STATE, 1)
    step_size = jax.nn.softplus(step_raw[0])
    cum_log = jnp.cumsum(-decay_rate[None, :] * step_size, axis=0)
    seg_row = segment[0]
    block_count = stream_len // BLOCK
    x_blk = inner_x[0].reshape(block_count, BLOCK, dev_heads, HEAD)
    cum_blk = cum_log.reshape(block_count, BLOCK, dev_heads)
    step_blk = step_size.reshape(block_count, BLOCK, dev_heads)
    seg_blk = seg_row.reshape(block_count, BLOCK)
    b_blk = b_cols.reshape(block_count, BLOCK, STATE)
    c_blk = c_cols.reshape(block_count, BLOCK, STATE)
    positions = jnp.arange(BLOCK)
    scores = jnp.einsum("btn,bsn->bts", c_blk, b_blk, preferred_element_type=jnp.float32)
    causal_mask = (positions[None, None, :] <= positions[None, :, None]) & (
        seg_blk[:, :, None] == seg_blk[:, None, :]
    )
    cum_t = cum_blk.transpose(0, 2, 1)
    log_gap = cum_t[:, :, :, None] - cum_t[:, :, None, :]
    weights = (
        jnp.exp(jnp.where(causal_mask[:, None], log_gap, -jnp.inf))
        * step_blk.transpose(0, 2, 1)[:, :, None, :]
        * scores[:, None]
    )
    intra_part = split_einsum("bhts,bshp->bthp", weights, x_blk)
    last_seg = seg_blk[:, -1]
    last_cum = cum_blk[:, -1]
    pull_back = (
        jnp.exp(last_cum[:, None, :] - cum_blk)
        * step_blk
        * (seg_blk == last_seg[:, None]).astype(jnp.float32)[:, :, None]
    )
    added = split_einsum("bshp,bsn->bhpn", pull_back[:, :, :, None] * x_blk, b_blk)
    prev_cum = jnp.concatenate([jnp.zeros((1, dev_heads), jnp.float32), last_cum[:-1]], axis=0)
    prev_seg = jnp.concatenate([jnp.full((1,), -1, seg_row.dtype), last_seg[:-1]], axis=0)
    blocks = jnp.arange(block_count)
    earlier = blocks[None, :] < blocks[:, None]
    mix_ok = earlier & (last_seg[None, :] == prev_seg[:, None])
    mix_gap = prev_cum[:, None, :] - last_cum[None, :, :]
    mix = jnp.exp(jnp.where(mix_ok[:, :, None], mix_gap, -jnp.inf))
    carried = jnp.sum(mix[:, :, :, None, None] * added[None], axis=1)
    live_rows = (seg_blk == prev_seg[:, None]).astype(jnp.float32)
    carry_decay = jnp.exp(cum_blk - prev_cum[:, None, :]) * live_rows[:, :, None]
    carry_part = split_einsum("bhpn,btn->bthp", carried, c_blk) * carry_decay[:, :, :, None]
    outputs = intra_part + carry_part + skip_gain[None, None, :, None] * x_blk.astype(jnp.float32)
    mixer_y = outputs.reshape(stream_len, dev_width)
    members = (seg_row[None, :] == jnp.arange(REQS)[:, None]).astype(jnp.float32)
    end_index = (
        jnp.sum((seg_row[None, :] <= jnp.arange(REQS)[:, None]).astype(jnp.int32), axis=1) - 1
    )
    at_end = (jnp.arange(stream_len)[None, :] == end_index[:, None]).astype(jnp.float32)
    end_cum = jnp.dot(at_end, cum_log, precision=HIGHEST)
    seg_end_cum = jnp.dot(members.T, end_cum, precision=HIGHEST)
    pull_all = jnp.exp(seg_end_cum - cum_log) * step_size
    weighted = (inner_x[0].reshape(stream_len, dev_heads, HEAD) * pull_all[:, :, None]).reshape(
        stream_len, dev_width
    )
    masked_b = (
        (members.astype(jnp.bfloat16)[:, :, None] * b_cols[None])
        .transpose(1, 0, 2)
        .reshape(stream_len, REQS * STATE)
    )
    finals = split_einsum("tc,tk->ck", weighted, masked_b)
    finals = (
        finals.reshape(dev_heads, HEAD, REQS, STATE)
        .transpose(2, 0, 1, 3)
        .reshape(REQS, dev_heads * HEAD * STATE)
    )
    gated = mixer_y * jax.nn.silu(gate_z[0].astype(jnp.float32))
    sum_sq = jnp.sum(gated * gated, axis=1)
    group_stat = lax.all_gather(sum_sq, GROUP_MATES, tiled=True)
    mean_sq = jnp.sum(group_stat.reshape(-1, stream_len), axis=0) / (INNER // NGROUPS)
    rounded = (gated * lax.rsqrt(mean_sq + 1e-05)[:, None] * norm_gain[None, :]).astype(
        jnp.bfloat16
    )
    sizes = [lax.axis_size(name) for name in TENSOR]
    rows = stream_len // (sizes[0] * sizes[1] * sizes[2] * sizes[3])
    reordered = (
        rounded.reshape(sizes[0], sizes[1], sizes[2], sizes[3], rows, dev_width)
        .transpose(0, 1, 3, 2, 4, 5)
        .reshape(stream_len, dev_width)
    )
    partial = jnp.dot(reordered, out_weight, preferred_element_type=jnp.float32).astype(jnp.bfloat16)
    near = lax.psum_scatter(partial, NEAR_FIRST, scatter_dimension=0, tiled=True)
    mixed = near
    dp_idx = lax.axis_index("dp")
    dp_size = lax.axis_size("dp")
    own_slots = lax.dynamic_slice_in_dim(cache_slot, dp_idx, 1, 0)[0]
    dest_hot = ((own_slots // REQS)[:, None] == jnp.arange(dp_size)[None, :]).astype(jnp.float32)
    outbound = jnp.dot(dest_hot.T, finals, precision=HIGHEST).reshape(
        dp_size, dev_heads, HEAD * STATE
    )
    inbound = lax.all_to_all(
        outbound.astype(jnp.bfloat16), "dp", split_axis=0, concat_axis=0, tiled=True
    ).astype(outbound.dtype)
    near, inbound = lax.optimization_barrier((mixed, inbound))
    far_idx = lax.axis_index(FAR_LAST)
    half = near.shape[0] // 2
    keep = lax.dynamic_slice_in_dim(near, far_idx * half, half, 0)
    send = lax.dynamic_slice_in_dim(near, (1 - far_idx) * half, half, 0)
    got = lax.ppermute(send, FAR_LAST, perm=[(0, 1), (1, 0)])
    projected = (keep.astype(jnp.float32) + got.astype(jnp.float32)).astype(jnp.bfloat16)
    mixed = projected[None]
    wanted = dp_idx * REQS + jnp.arange(REQS)
    take_hot = jnp.any(cache_slot[:, :, None] == wanted[None, None, :], axis=1).astype(jnp.float32)
    cache = jnp.dot(
        take_hot.T, inbound.reshape(dp_size, dev_heads * HEAD * STATE), precision=HIGHEST
    )
    return (mixed, cache.reshape(REQS, dev_heads, HEAD * STATE))


def solution(mesh):
    dp_size, tensor_size = mesh.devices.shape
    groups = NGROUPS
    rest = tensor_size // (2 * 2 * groups)
    split = Mesh(
        mesh.devices.reshape(dp_size, groups, rest, 2, 2), ("dp",) + TENSOR
    )
    tp = TENSOR
    in_specs = (
        P("dp", None, tp),
        P("dp", None, tp),
        P("dp", None, None),
        P("dp", None, None),
        P("dp", None, tp),
        P(tp),
        P(tp),
        P(tp),
        P(tp, None),
        P("dp", None),
        P(),
    )
    out_specs = (P("dp", tp, None), P("dp", tp, None))
    return jax.shard_map(local, mesh=split, in_specs=in_specs, out_specs=out_specs, check_vma=False)
```
